1024 devices in a mesh: seq: 64 (over z, x), ctx: 16 (over y, core).
Axes of the slice: x: 4, y: 8, z: 16, core: 2. Of those that a mesh axis runs over, the one named last changes fastest.
Arguments:
- queries: bfloat16 [16, 4096, 8192], P('ctx', 'seq'), may hold values from -36 to 36
- keys: bfloat16 [16, 4096, 1024], P('ctx', 'seq'), may hold values from -6 to 6
- values: bfloat16 [16, 4096, 1024], P('ctx', 'seq'), may hold values from -6 to 6
- columns: int32 [64, 8], replicated, may hold values from 0 to 511, as said below
- offsets: int32 [64, 4], replicated, may hold values from 0 to 7, as said below
Outputs:
- attended: bfloat16 [16, 4096, 8192], P('ctx', 'seq')
The draws below stay inside these ranges and needn't reach their ends.
Inputs may be any that keep to these rules, and one draw needn't show every extreme that they name: `columns`: each row holds 8 different block numbers. For every head, at most 2 of its blocks lie in one range of 32 blocks that starts at a multiple of 32, and some range holds exactly 2 of them. Each row holds 4 different offsets, the first of them 0.
All inputs are finite; a program needn't handle non-finite values.
Results may differ from the reference program's by a relative error of at most 0.0046.
Values may be sent and summed in bfloat16 or wider, within the bound.
No kernel may reach another device: no remote copies, remote signals or barrier semaphores. Data moves between devices by JAX's collectives and lax.ppermute only.
A program may use at most 32 MiB of HBM per device.

```python
import math
import jax
import jax.numpy as jnp
from jax import lax

HD = 128
BLK = 128
G = 8
H = 64
KVH = 8
SPANS = 16
L_CH = 4096
SEQ_LEN = 65536
BPC = 32
BAND = 8
NS = 4
VCAP = 2
NV = 8


def shared_keys(key):
    sub_key = jax.random.fold_in(key, 7)
    base = jnp.clip(jax.random.normal(sub_key, (SPANS, L_CH, KVH, HD), jnp.float32), -6.0, 6.0)
    return base


def draw_keys(key, part):
    return shared_keys(key).reshape(SPANS, L_CH, KVH * HD).astype(jnp.bfloat16)


def draw_queries(key, part):
    sub_key = jax.random.fold_in(key, 13)
    drawn = jnp.clip(jax.random.normal(sub_key, (SPANS, L_CH, H, HD), jnp.float32), -6.0, 6.0)
    return drawn.reshape(SPANS, L_CH, H * HD).astype(jnp.bfloat16)


def one_columns(sub_key):
    first_key, second_key, third_key = jax.random.split(sub_key, 3)
    heavy = jax.random.randint(first_key, (), 0, SPANS)
    others = (heavy + 1 + jax.random.permutation(second_key, SPANS - 1)) % SPANS
    order = jnp.arange(NV, dtype=jnp.int32)
    spread = jnp.maximum(order - VCAP, 0)
    owner = jnp.where(order < VCAP, heavy, others[spread % (SPANS - 1)])
    within = jnp.where(order < VCAP, order, spread // (SPANS - 1))
    start = jax.random.randint(third_key, (), 0, BPC)
    return (owner * BPC + (start + within) % BPC).astype(jnp.int32)


def draw_columns(key, part):
    return jax.vmap(one_columns)(jax.random.split(key, H))


def one_offsets(sub_key):
    rest = jax.random.permutation(sub_key, BAND - 1) + 1
    return jnp.concatenate([jnp.zeros((1,), jnp.int32), rest[:NS - 1].astype(jnp.int32)])


def draw_offsets(key, part):
    return jax.vmap(one_offsets)(jax.random.split(jax.random.fold_in(key, 3), H))


def block_scale(stream_key, extent, pieces, smallest, top_value):
    gain = 1.0
    for axis_at, blocks in pieces:
        heights = jax.random.uniform(jax.random.fold_in(jax.random.fold_in(stream_key, 6), axis_at), (blocks,), jnp.float32, smallest / len(pieces), top_value / len(pieces))
        gain = gain * jnp.repeat(jnp.exp(heights), extent[axis_at] // blocks).reshape((-1,) + (1,) * (len(extent) - 1 - axis_at))
    return gain


def gaussian(key, shape, width, reach, cuts=(), kind=jnp.bfloat16):
    values = jax.random.normal(key, shape, jnp.float32) * width
    if len(cuts) > 0:
        values = block_scale(key, shape, cuts, -0.22, 0.18) * values
    return jnp.clip(values, min=-reach, max=reach).astype(kind)


def setup_inputs(seed: int = 0) -> dict:
    streams_of = jax.random.split(jax.random.key(seed), 6)
    return {
        "queries": draw_queries(jax.random.fold_in(streams_of[5], 71), 0),
        "keys": draw_keys(jax.random.fold_in(streams_of[5], 71), 0),
        "values": gaussian(streams_of[2], (SPANS, L_CH, KVH * HD), 1.0, 6.0, ((0, 16), (1, 64))),
        "columns": draw_columns(jax.random.fold_in(streams_of[5], 71), 0),
        "offsets": draw_offsets(jax.random.fold_in(streams_of[5], 71), 0),
    }


def head_output(head_queries, head_keys, head_values, vertical, slashes):
    block_count = head_queries.shape[0] // BLK
    query_blocks = head_queries.reshape(block_count, BLK, HD)
    key_blocks = head_keys.reshape(block_count, BLK, HD)
    value_blocks = head_values.reshape(block_count, BLK, HD)
    row_index = jnp.arange(BLK, dtype=jnp.int32)
    keep_vertical = jnp.ones((vertical.shape[0],), dtype=bool)
    score_scale = 1.0 / math.sqrt(HD)

    def one_block(query_block):
        slash_blocks = (query_block - slashes).astype(jnp.int32)
        repeated = jnp.any(slash_blocks[:, None] == vertical[None, :], axis=1)
        candidates = jnp.concatenate([vertical.astype(jnp.int32), slash_blocks]).astype(jnp.int32)
        usable = jnp.concatenate([keep_vertical, jnp.logical_not(repeated)])
        usable = usable & (candidates >= 0) & (candidates <= query_block)
        clipped = jnp.clip(candidates, 0, block_count - 1).astype(jnp.int32)
        nearby_keys = key_blocks[clipped].reshape(-1, HD)
        nearby_values = value_blocks[clipped].reshape(-1, HD)
        block_queries = query_blocks[query_block]
        scores = jnp.dot(block_queries, nearby_keys.T, preferred_element_type=jnp.float32) * score_scale
        visible = (candidates < query_block)[None, :, None] | (row_index[None, None, :] <= row_index[:, None, None])
        allowed = (usable[None, :, None] & visible).reshape(BLK, -1)
        scores = jnp.where(allowed, scores, -1e+30)
        row_max = lax.optimization_barrier(jnp.max(scores, axis=1, keepdims=True))
        weights = jnp.where(allowed, jnp.exp(scores - row_max), 0.0)
        denominator = lax.optimization_barrier(jnp.sum(weights, axis=1, keepdims=True))
        weighted = jnp.dot(weights.astype(jnp.bfloat16), nearby_values, preferred_element_type=jnp.float32)
        return (weighted / denominator).astype(jnp.bfloat16)
    return lax.map(one_block, jnp.arange(block_count, dtype=jnp.int32))

def reference(queries, keys, values, columns, offsets):
    all_queries = queries.reshape(SEQ_LEN, H, HD)
    all_keys = keys.reshape(SEQ_LEN, KVH, HD)
    all_values = values.reshape(SEQ_LEN, KVH, HD)

    def one_head(head_index):
        shared = head_index // G
        head_queries = all_queries[:, head_index]
        head_keys = all_keys[:, shared]
        head_values = all_values[:, shared]
        result = head_output(head_queries, head_keys, head_values, columns[head_index], offsets[head_index])
        return result.reshape(SEQ_LEN, HD)
    outputs = lax.map(one_head, jnp.arange(H, dtype=jnp.int32))
    return jnp.transpose(outputs, (1, 0, 2)).reshape(SPANS, L_CH, H * HD)
```

```python
import functools
import math

import jax
import jax.numpy as jnp
from jax import lax
from jax.experimental import pallas as pl
from jax.experimental.pallas import tpu as pltpu
from jax.sharding import PartitionSpec as P

BLK = 128
BACK = 7
NEVER = -4 * BLK


def from_behind(block, axis, distance):
    devices = range(lax.axis_size(axis))
    route = [(i - distance, i) for i in devices if i - distance in devices]
    return lax.ppermute(block, axis, route)


def attend_kernel(index_ref, bound_ref, q_ref, pool_ref, o_ref, score_ref, *, candidates, head_dim):
    block = pl.program_id(0)
    scale = 1.0 / math.sqrt(head_dim)
    queries = q_ref[...]
    row = lax.broadcasted_iota(jnp.int32, (BLK, BLK), 0)
    col = lax.broadcasted_iota(jnp.int32, (BLK, BLK), 1)
    offset = col - row
    running = None
    for k in range(candidates):
        slot = index_ref[block * candidates + k]
        bound = bound_ref[block * candidates + k]
        keys = pool_ref[slot, :, :head_dim]
        scores = (
            lax.dot_general(
                queries, keys, (((1,), (1,)), ((), ())), preferred_element_type=jnp.float32
            )
            * scale
        )
        scores = jnp.where(offset <= bound, scores, -1e30)
        score_ref[k] = scores
        running = scores if running is None else jnp.maximum(running, scores)
    row_max = jnp.max(running, axis=1, keepdims=True)
    total = None
    acc = None
    for k in range(candidates):
        slot = index_ref[block * candidates + k]
        bound = bound_ref[block * candidates + k]
        values = pool_ref[slot, :, head_dim:]
        weights = jnp.where(offset <= bound, jnp.exp(score_ref[k] - row_max), 0.0)
        total = weights if total is None else total + weights
        part = jnp.dot(weights.astype(jnp.bfloat16), values, preferred_element_type=jnp.float32)
        acc = part if acc is None else acc + part
    denominator = jnp.sum(total, axis=1, keepdims=True)
    o_ref[...] = (acc / denominator).astype(o_ref.dtype)


def attend(head_queries, key_pool, pool_index, bounds):
    range_len, head_dim = head_queries.shape
    blocks = range_len // BLK
    candidates = pool_index.shape[1]
    pool_size = key_pool.shape[0]
    kernel = functools.partial(attend_kernel, candidates=candidates, head_dim=head_dim)
    grid_spec = pltpu.PrefetchScalarGridSpec(
        num_scalar_prefetch=2,
        grid=(blocks,),
        in_specs=[
            pl.BlockSpec((BLK, head_dim), lambda i, *_: (i, 0)),
            pl.BlockSpec((pool_size, BLK, 2 * head_dim), lambda i, *_: (0, 0, 0)),
        ],
        out_specs=pl.BlockSpec((BLK, head_dim), lambda i, *_: (i, 0)),
        scratch_shapes=[pltpu.VMEM((candidates, BLK, BLK), jnp.float32)],
    )
    flops = 4 * range_len * candidates * BLK * head_dim
    return pl.pallas_call(
        kernel,
        grid_spec=grid_spec,
        out_shape=jax.ShapeDtypeStruct((range_len, head_dim), jnp.bfloat16),
        compiler_params=pltpu.CompilerParams(dimension_semantics=("arbitrary",)),
        cost_estimate=pl.CostEstimate(
            flops=flops,
            transcendentals=range_len * candidates * BLK,
            bytes_accessed=2 * range_len * head_dim * 2 + key_pool.size * 2,
        ),
    )(pool_index.reshape(-1), bounds.reshape(-1), head_queries, key_pool)


def shards(queries, keys, values, columns, offsets):
    tokens_dev = queries.shape[1]
    seq_count = lax.axis_size("seq")
    head_dim = queries.shape[2] // seq_count
    kv_heads = keys.shape[2] // head_dim
    group_size = seq_count // kv_heads
    vertical_count = columns.shape[1]
    local_queries = queries.reshape(tokens_dev, seq_count, head_dim)
    local_pairs = jnp.concatenate(
        [
            keys.reshape(tokens_dev, kv_heads, 1, head_dim),
            values.reshape(tokens_dev, kv_heads, 1, head_dim),
        ],
        axis=3,
    )
    local_pairs = jnp.broadcast_to(
        local_pairs, (tokens_dev, kv_heads, group_size, 2 * head_dim)
    ).reshape(tokens_dev, seq_count, 2 * head_dim)
    head_queries = lax.all_to_all(local_queries, "seq", split_axis=1, concat_axis=0, tiled=True)
    head_pairs = lax.all_to_all(local_pairs, "seq", split_axis=1, concat_axis=0, tiled=True)
    range_len = tokens_dev * seq_count
    blocks_slab = range_len // BLK
    head_queries = head_queries.reshape(range_len, head_dim)
    own_pairs = head_pairs.reshape(range_len, 2 * head_dim)
    own_blocks = own_pairs.reshape(blocks_slab, BLK, 2 * head_dim)
    head_index = lax.axis_index("seq")
    range_index = lax.axis_index("ctx")
    vertical = lax.dynamic_index_in_dim(columns, head_index, 0, keepdims=False)
    slashes = lax.dynamic_index_in_dim(offsets, head_index, 0, keepdims=False)
    first_block = range_index * blocks_slab
    local_index = vertical - first_block
    owned_mask = (local_index >= 0) & (local_index < blocks_slab)
    clipped_local = jnp.clip(local_index, 0, blocks_slab - 1)
    taken_blocks = own_blocks[clipped_local]
    slot_table = jnp.where(owned_mask[:, None, None], taken_blocks, jnp.zeros((), jnp.bfloat16))
    vertical_pairs = lax.psum(slot_table, "ctx")
    previous = from_behind(own_pairs[range_len - BACK * BLK :], "ctx", 1)
    key_pool = jnp.concatenate(
        [previous.reshape(BACK, BLK, 2 * head_dim), own_blocks, vertical_pairs], axis=0
    )
    pool_size = key_pool.shape[0]
    pool_base = first_block - BACK
    query_index = first_block + jnp.arange(blocks_slab, dtype=jnp.int32)
    slash_blocks = query_index[:, None] - slashes[None, :]
    repeated = jnp.any(slash_blocks[:, :, None] == vertical[None, None, :], axis=2)
    candidates = jnp.concatenate(
        [jnp.broadcast_to(vertical[None, :], (blocks_slab, vertical_count)), slash_blocks], axis=1
    )
    usable = jnp.concatenate(
        [jnp.ones((blocks_slab, vertical_count), dtype=bool), jnp.logical_not(repeated)], axis=1
    )
    usable = usable & (candidates >= 0) & (candidates <= query_index[:, None])
    strict = candidates < query_index[:, None]
    bounds = jnp.where(usable, jnp.where(strict, BLK, 0), NEVER).astype(jnp.int32)
    vertical_slots = jnp.broadcast_to(
        (BACK + blocks_slab + jnp.arange(vertical_count, dtype=jnp.int32))[None, :],
        (blocks_slab, vertical_count),
    )
    pool_index = jnp.concatenate([vertical_slots, slash_blocks - pool_base], axis=1)
    pool_index = jnp.clip(pool_index, 0, pool_size - 1).astype(jnp.int32)
    head_output = attend(head_queries, key_pool, pool_index, bounds).reshape(range_len, 1, head_dim)
    returned = lax.all_to_all(head_output, "seq", split_axis=0, concat_axis=1, tiled=True)
    return returned.reshape(1, tokens_dev, seq_count * head_dim)


def solution(mesh):
    placed = (P("ctx", "seq", None), P("ctx", "seq", None), P("ctx", "seq", None), P(), P())
    return jax.shard_map(
        shards, mesh=mesh, in_specs=placed, out_specs=P("ctx", "seq", None), check_vma=False
    )
```

```python
import functools
import math

import jax
import jax.numpy as jnp
from jax import lax
from jax.experimental import pallas as pl
from jax.experimental.pallas import tpu as pltpu
from jax.sharding import PartitionSpec as P

BLK = 128
BACK = 7
NEVER = -4 * BLK
VCAP = 2


def from_behind(block, axis, distance):
    devices = range(lax.axis_size(axis))
    route = [(i - distance, i) for i in devices if i - distance in devices]
    return lax.ppermute(block, axis, route)


def attend_kernel(index_ref, bound_ref, q_ref, pool_ref, o_ref, score_ref, *, candidates, head_dim):
    block = pl.program_id(0)
    scale = 1.0 / math.sqrt(head_dim)
    queries = q_ref[...]
    row = lax.broadcasted_iota(jnp.int32, (BLK, BLK), 0)
    col = lax.broadcasted_iota(jnp.int32, (BLK, BLK), 1)
    offset = col - row
    running = None
    for k in range(candidates):
        slot = index_ref[block * candidates + k]
        bound = bound_ref[block * candidates + k]
        keys = pool_ref[slot, :, :head_dim]
        scores = (
            lax.dot_general(
                queries, keys, (((1,), (1,)), ((), ())), preferred_element_type=jnp.float32
            )
            * scale
        )
        scores = jnp.where(offset <= bound, scores, -1e30)
        score_ref[k] = scores
        running = scores if running is None else jnp.maximum(running, scores)
    row_max = jnp.max(running, axis=1, keepdims=True)
    total = None
    acc = None
    for k in range(candidates):
        slot = index_ref[block * candidates + k]
        bound = bound_ref[block * candidates + k]
        values = pool_ref[slot, :, head_dim:]
        weights = jnp.where(offset <= bound, jnp.exp(score_ref[k] - row_max), 0.0)
        total = weights if total is None else total + weights
        part = jnp.dot(weights.astype(jnp.bfloat16), values, preferred_element_type=jnp.float32)
        acc = part if acc is None else acc + part
    denominator = jnp.sum(total, axis=1, keepdims=True)
    o_ref[...] = (acc / denominator).astype(o_ref.dtype)


def attend(head_queries, key_pool, pool_index, bounds):
    range_len, head_dim = head_queries.shape
    blocks = range_len // BLK
    candidates = pool_index.shape[1]
    pool_size = key_pool.shape[0]
    kernel = functools.partial(attend_kernel, candidates=candidates, head_dim=head_dim)
    grid_spec = pltpu.PrefetchScalarGridSpec(
        num_scalar_prefetch=2,
        grid=(blocks,),
        in_specs=[
            pl.BlockSpec((BLK, head_dim), lambda i, *_: (i, 0)),
            pl.BlockSpec((pool_size, BLK, 2 * head_dim), lambda i, *_: (0, 0, 0)),
        ],
        out_specs=pl.BlockSpec((BLK, head_dim), lambda i, *_: (i, 0)),
        scratch_shapes=[pltpu.VMEM((candidates, BLK, BLK), jnp.float32)],
    )
    flops = 4 * range_len * candidates * BLK * head_dim
    return pl.pallas_call(
        kernel,
        grid_spec=grid_spec,
        out_shape=jax.ShapeDtypeStruct((range_len, head_dim), jnp.bfloat16),
        compiler_params=pltpu.CompilerParams(dimension_semantics=("arbitrary",)),
        cost_estimate=pl.CostEstimate(
            flops=flops,
            transcendentals=range_len * candidates * BLK,
            bytes_accessed=2 * range_len * head_dim * 2 + key_pool.size * 2,
        ),
    )(pool_index.reshape(-1), bounds.reshape(-1), head_queries, key_pool)


def shards(queries, keys, values, columns, offsets):
    tokens_dev = queries.shape[1]
    seq_count = lax.axis_size("seq")
    head_dim = queries.shape[2] // seq_count
    kv_heads = keys.shape[2] // head_dim
    group_size = seq_count // kv_heads
    vertical_count = columns.shape[1]
    local_queries = queries.reshape(tokens_dev, seq_count, head_dim)
    local_pairs = jnp.concatenate(
        [
            keys.reshape(tokens_dev, kv_heads, 1, head_dim),
            values.reshape(tokens_dev, kv_heads, 1, head_dim),
        ],
        axis=3,
    )
    local_pairs = jnp.broadcast_to(
        local_pairs, (tokens_dev, kv_heads, group_size, 2 * head_dim)
    ).reshape(tokens_dev, seq_count, 2 * head_dim)
    head_queries = lax.all_to_all(local_queries, "seq", split_axis=1, concat_axis=0, tiled=True)
    head_pairs = lax.all_to_all(local_pairs, "seq", split_axis=1, concat_axis=0, tiled=True)
    range_len = tokens_dev * seq_count
    blocks_slab = range_len // BLK
    head_queries = head_queries.reshape(range_len, head_dim)
    own_pairs = head_pairs.reshape(range_len, 2 * head_dim)
    own_blocks = own_pairs.reshape(blocks_slab, BLK, 2 * head_dim)
    head_index = lax.axis_index("seq")
    range_index = lax.axis_index("ctx")
    vertical = lax.dynamic_index_in_dim(columns, head_index, 0, keepdims=False)
    slashes = lax.dynamic_index_in_dim(offsets, head_index, 0, keepdims=False)
    first_block = range_index * blocks_slab
    owner = vertical // blocks_slab
    earlier = jnp.arange(vertical_count)[None, :] < jnp.arange(vertical_count)[:, None]
    rank = jnp.sum(earlier & (owner[None, :] == owner[:, None]), axis=1)
    rank = jnp.clip(rank, 0, VCAP - 1)
    held = (owner[None, :] == range_index) & (rank[None, :] == jnp.arange(VCAP)[:, None])
    local_index = jnp.sum(jnp.where(held, vertical[None, :] - first_block, 0), axis=1)
    taken_blocks = own_blocks[jnp.clip(local_index, 0, blocks_slab - 1)]
    vertical_pairs = lax.all_gather(taken_blocks, "ctx", tiled=True)
    previous = from_behind(own_pairs[range_len - BACK * BLK :], "ctx", 1)
    key_pool = jnp.concatenate(
        [previous.reshape(BACK, BLK, 2 * head_dim), own_blocks, vertical_pairs], axis=0
    )
    pool_size = key_pool.shape[0]
    pool_base = first_block - BACK
    query_index = first_block + jnp.arange(blocks_slab, dtype=jnp.int32)
    slash_blocks = query_index[:, None] - slashes[None, :]
    repeated = jnp.any(slash_blocks[:, :, None] == vertical[None, None, :], axis=2)
    candidates = jnp.concatenate(
        [jnp.broadcast_to(vertical[None, :], (blocks_slab, vertical_count)), slash_blocks], axis=1
    )
    usable = jnp.concatenate(
        [jnp.ones((blocks_slab, vertical_count), dtype=bool), jnp.logical_not(repeated)], axis=1
    )
    usable = usable & (candidates >= 0) & (candidates <= query_index[:, None])
    strict = candidates < query_index[:, None]
    bounds = jnp.where(usable, jnp.where(strict, BLK, 0), NEVER).astype(jnp.int32)
    vertical_slots = jnp.broadcast_to(
        (BACK + blocks_slab + owner * VCAP + rank).astype(jnp.int32)[None, :],
        (blocks_slab, vertical_count),
    )
    pool_index = jnp.concatenate([vertical_slots, slash_blocks - pool_base], axis=1)
    pool_index = jnp.clip(pool_index, 0, pool_size - 1).astype(jnp.int32)
    head_output = attend(head_queries, key_pool, pool_index, bounds).reshape(range_len, 1, head_dim)
    returned = lax.all_to_all(head_output, "seq", split_axis=0, concat_axis=1, tiled=True)
    return returned.reshape(1, tokens_dev, seq_count * head_dim)


def solution(mesh):
    placed = (P("ctx", "seq", None), P("ctx", "seq", None), P("ctx", "seq", None), P(), P())
    return jax.shard_map(
        shards, mesh=mesh, in_specs=placed, out_specs=P("ctx", "seq", None), check_vma=False
    )
```

```python
import functools
import math

import jax
import jax.numpy as jnp
from jax import lax
from jax.experimental import pallas as pl
from jax.experimental.pallas import tpu as pltpu
from jax.sharding import Mesh, PartitionSpec as P

BLK = 128
SEQ = ("grp", "mem")
BACK = 7
NEVER = -4 * BLK
VCAP = 2


def from_behind(block, axis, distance):
    devices = range(lax.axis_size(axis))
    route = [(i - distance, i) for i in devices if i - distance in devices]
    return lax.ppermute(block, axis, route)


def attend_kernel(index_ref, bound_ref, q_ref, pool_ref, o_ref, score_ref, *, candidates, head_dim):
    block = pl.program_id(0)
    scale = 1.0 / math.sqrt(head_dim)
    queries = q_ref[...]
    row = lax.broadcasted_iota(jnp.int32, (BLK, BLK), 0)
    col = lax.broadcasted_iota(jnp.int32, (BLK, BLK), 1)
    offset = col - row
    running = None
    for k in range(candidates):
        slot = index_ref[block * candidates + k]
        bound = bound_ref[block * candidates + k]
        keys = pool_ref[slot, :, :head_dim]
        scores = (
            lax.dot_general(
                queries, keys, (((1,), (1,)), ((), ())), preferred_element_type=jnp.float32
            )
            * scale
        )
        scores = jnp.where(offset <= bound, scores, -1e30)
        score_ref[k] = scores
        running = scores if running is None else jnp.maximum(running, scores)
    row_max = jnp.max(running, axis=1, keepdims=True)
    total = None
    acc = None
    for k in range(candidates):
        slot = index_ref[block * candidates + k]
        bound = bound_ref[block * candidates + k]
        values = pool_ref[slot, :, head_dim:]
        weights = jnp.where(offset <= bound, jnp.exp(score_ref[k] - row_max), 0.0)
        total = weights if total is None else total + weights
        part = jnp.dot(weights.astype(jnp.bfloat16), values, preferred_element_type=jnp.float32)
        acc = part if acc is None else acc + part
    denominator = jnp.sum(total, axis=1, keepdims=True)
    o_ref[...] = (acc / denominator).astype(o_ref.dtype)


def attend(head_queries, key_pool, pool_index, bounds):
    range_len, head_dim = head_queries.shape
    blocks = range_len // BLK
    candidates = pool_index.shape[1]
    pool_size = key_pool.shape[0]
    kernel = functools.partial(attend_kernel, candidates=candidates, head_dim=head_dim)
    grid_spec = pltpu.PrefetchScalarGridSpec(
        num_scalar_prefetch=2,
        grid=(blocks,),
        in_specs=[
            pl.BlockSpec((BLK, head_dim), lambda i, *_: (i, 0)),
            pl.BlockSpec((pool_size, BLK, 2 * head_dim), lambda i, *_: (0, 0, 0)),
        ],
        out_specs=pl.BlockSpec((BLK, head_dim), lambda i, *_: (i, 0)),
        scratch_shapes=[pltpu.VMEM((candidates, BLK, BLK), jnp.float32)],
    )
    flops = 4 * range_len * candidates * BLK * head_dim
    return pl.pallas_call(
        kernel,
        grid_spec=grid_spec,
        out_shape=jax.ShapeDtypeStruct((range_len, head_dim), jnp.bfloat16),
        compiler_params=pltpu.CompilerParams(dimension_semantics=("arbitrary",)),
        cost_estimate=pl.CostEstimate(
            flops=flops,
            transcendentals=range_len * candidates * BLK,
            bytes_accessed=2 * range_len * head_dim * 2 + key_pool.size * 2,
        ),
    )(pool_index.reshape(-1), bounds.reshape(-1), head_queries, key_pool)


def shards(queries, keys, values, columns, offsets):
    tokens_dev = queries.shape[1]
    seq_count = lax.axis_size(SEQ)
    head_dim = queries.shape[2] // seq_count
    kv_heads = keys.shape[2] // head_dim
    vertical_count = columns.shape[1]
    local_queries = queries.reshape(tokens_dev, seq_count, head_dim)
    local_pairs = jnp.concatenate(
        [
            keys.reshape(tokens_dev, kv_heads, head_dim),
            values.reshape(tokens_dev, kv_heads, head_dim),
        ],
        axis=2,
    )
    group_pairs = lax.all_to_all(local_pairs, "grp", split_axis=1, concat_axis=0, tiled=True)
    group_pairs = lax.all_gather(group_pairs, "mem", axis=0, tiled=False)
    head_queries = lax.all_to_all(local_queries, SEQ, split_axis=1, concat_axis=0, tiled=True)
    members = group_pairs.shape[0]
    group_pairs = group_pairs.reshape(members, kv_heads, tokens_dev, 2 * head_dim)
    head_pairs = jnp.transpose(group_pairs, (1, 0, 2, 3))
    range_len = tokens_dev * seq_count
    blocks_slab = range_len // BLK
    head_queries = head_queries.reshape(range_len, head_dim)
    own_pairs = head_pairs.reshape(range_len, 2 * head_dim)
    own_blocks = own_pairs.reshape(blocks_slab, BLK, 2 * head_dim)
    head_index = lax.axis_index(SEQ)
    range_index = lax.axis_index("ctx")
    vertical = lax.dynamic_index_in_dim(columns, head_index, 0, keepdims=False)
    slashes = lax.dynamic_index_in_dim(offsets, head_index, 0, keepdims=False)
    first_block = range_index * blocks_slab
    owner = vertical // blocks_slab
    earlier = jnp.arange(vertical_count)[None, :] < jnp.arange(vertical_count)[:, None]
    rank = jnp.sum(earlier & (owner[None, :] == owner[:, None]), axis=1)
    rank = jnp.clip(rank, 0, VCAP - 1)
    held = (owner[None, :] == range_index) & (rank[None, :] == jnp.arange(VCAP)[:, None])
    local_index = jnp.sum(jnp.where(held, vertical[None, :] - first_block, 0), axis=1)
    taken_blocks = own_blocks[jnp.clip(local_index, 0, blocks_slab - 1)]
    vertical_pairs = lax.all_gather(taken_blocks, "ctx", tiled=True)
    previous = from_behind(own_pairs[range_len - BACK * BLK :], "ctx", 1)
    key_pool = jnp.concatenate(
        [previous.reshape(BACK, BLK, 2 * head_dim), own_blocks, vertical_pairs], axis=0
    )
    pool_size = key_pool.shape[0]
    pool_base = first_block - BACK
    query_index = first_block + jnp.arange(blocks_slab, dtype=jnp.int32)
    slash_blocks = query_index[:, None] - slashes[None, :]
    repeated = jnp.any(slash_blocks[:, :, None] == vertical[None, None, :], axis=2)
    candidates = jnp.concatenate(
        [jnp.broadcast_to(vertical[None, :], (blocks_slab, vertical_count)), slash_blocks], axis=1
    )
    usable = jnp.concatenate(
        [jnp.ones((blocks_slab, vertical_count), dtype=bool), jnp.logical_not(repeated)], axis=1
    )
    usable = usable & (candidates >= 0) & (candidates <= query_index[:, None])
    strict = candidates < query_index[:, None]
    bounds = jnp.where(usable, jnp.where(strict, BLK, 0), NEVER).astype(jnp.int32)
    vertical_slots = jnp.broadcast_to(
        (BACK + blocks_slab + owner * VCAP + rank).astype(jnp.int32)[None, :],
        (blocks_slab, vertical_count),
    )
    pool_index = jnp.concatenate([vertical_slots, slash_blocks - pool_base], axis=1)
    pool_index = jnp.clip(pool_index, 0, pool_size - 1).astype(jnp.int32)
    head_output = attend(head_queries, key_pool, pool_index, bounds).reshape(range_len, 1, head_dim)
    returned = lax.all_to_all(head_output, SEQ, split_axis=0, concat_axis=1, tiled=True)
    return returned.reshape(1, tokens_dev, seq_count * head_dim)


def solution(mesh):
    def run(queries, keys, values, columns, offsets):
        seq_count = mesh.shape["seq"]
        kv_heads = keys.shape[2] // (queries.shape[2] // seq_count)
        devices = mesh.devices.reshape(kv_heads, seq_count // kv_heads, mesh.shape["ctx"])
        split = Mesh(devices, ("grp", "mem", "ctx"))
        placed = P("ctx", SEQ, None)
        step = jax.shard_map(
            shards,
            mesh=split,
            in_specs=(placed, placed, placed, P(), P()),
            out_specs=placed,
            check_vma=False,
        )
        return step(queries, keys, values, columns, offsets)

    return run
```

```python
import functools
import math

import jax
import jax.numpy as jnp
from jax import lax
from jax.experimental import pallas as pl
from jax.experimental.pallas import tpu as pltpu
from jax.sharding import Mesh, PartitionSpec as P

BLK = 128
SEQ = ("grp", "mem")
BACK = 7
NEVER = -4 * BLK
VCAP = 2


def from_behind(block, axis, distance):
    devices = range(lax.axis_size(axis))
    route = [(i - distance, i) for i in devices if i - distance in devices]
    return lax.ppermute(block, axis, route)


def attend_kernel(
    index_ref, bound_ref, q_ref, pool_ref, o_ref, key_ref, value_ref, *, candidates, head_dim, per_step
):
    step = pl.program_id(0)
    scale = 1.0 / math.sqrt(head_dim)
    row = lax.broadcasted_iota(jnp.int32, (BLK, BLK), 0)
    col = lax.broadcasted_iota(jnp.int32, (BLK, BLK), 1)
    offset = col - row
    for part in range(per_step):
        block = step * per_step + part
        for k in range(candidates):
            slot = index_ref[block * candidates + k]
            key_ref[k * BLK : (k + 1) * BLK, :] = pool_ref[slot, :, :head_dim]
            value_ref[k * BLK : (k + 1) * BLK, :] = pool_ref[slot, :, head_dim:]
        queries = q_ref[part * BLK : (part + 1) * BLK, :]
        scores = (
            lax.dot_general(
                queries, key_ref[...], (((1,), (1,)), ((), ())), preferred_element_type=jnp.float32
            )
            * scale
        )
        masked = []
        for k in range(candidates):
            bound = bound_ref[block * candidates + k]
            masked.append(jnp.where(offset <= bound, scores[:, k * BLK : (k + 1) * BLK], -1e30))
        scores = jnp.concatenate(masked, axis=1)
        row_max = jnp.max(scores, axis=1, keepdims=True)
        weights = jnp.exp(scores - row_max)
        denominator = jnp.sum(weights, axis=1, keepdims=True)
        weighted = jnp.dot(
            weights.astype(jnp.bfloat16), value_ref[...], preferred_element_type=jnp.float32
        )
        o_ref[part * BLK : (part + 1) * BLK, :] = (weighted / denominator).astype(o_ref.dtype)


def attend(head_queries, key_pool, pool_index, bounds, per_step=2):
    range_len, head_dim = head_queries.shape
    blocks = range_len // BLK
    candidates = pool_index.shape[1]
    pool_size = key_pool.shape[0]
    kernel = functools.partial(
        attend_kernel, candidates=candidates, head_dim=head_dim, per_step=per_step
    )
    rows = per_step * BLK
    grid_spec = pltpu.PrefetchScalarGridSpec(
        num_scalar_prefetch=2,
        grid=(blocks // per_step,),
        in_specs=[
            pl.BlockSpec((rows, head_dim), lambda i, *_: (i, 0)),
            pl.BlockSpec((pool_size, BLK, 2 * head_dim), lambda i, *_: (0, 0, 0)),
        ],
        out_specs=pl.BlockSpec((rows, head_dim), lambda i, *_: (i, 0)),
        scratch_shapes=[
            pltpu.VMEM((candidates * BLK, head_dim), jnp.bfloat16),
            pltpu.VMEM((candidates * BLK, head_dim), jnp.bfloat16),
        ],
    )
    flops = 4 * range_len * candidates * BLK * head_dim
    return pl.pallas_call(
        kernel,
        grid_spec=grid_spec,
        out_shape=jax.ShapeDtypeStruct((range_len, head_dim), jnp.bfloat16),
        compiler_params=pltpu.CompilerParams(dimension_semantics=("arbitrary",)),
        cost_estimate=pl.CostEstimate(
            flops=flops,
            transcendentals=range_len * candidates * BLK,
            bytes_accessed=2 * range_len * head_dim * 2 + key_pool.size * 2,
        ),
    )(pool_index.reshape(-1), bounds.reshape(-1), head_queries, key_pool)


def shards(queries, keys, values, columns, offsets):
    tokens_dev = queries.shape[1]
    seq_count = lax.axis_size(SEQ)
    head_dim = queries.shape[2] // seq_count
    kv_heads = keys.shape[2] // head_dim
    vertical_count = columns.shape[1]
    local_queries = queries.reshape(tokens_dev, seq_count, head_dim)
    local_pairs = jnp.concatenate(
        [
            keys.reshape(tokens_dev, kv_heads, head_dim),
            values.reshape(tokens_dev, kv_heads, head_dim),
        ],
        axis=2,
    )
    group_pairs = lax.all_to_all(local_pairs, "grp", split_axis=1, concat_axis=0, tiled=True)
    group_pairs = lax.all_gather(group_pairs, "mem", axis=0, tiled=False)
    head_queries = lax.all_to_all(local_queries, SEQ, split_axis=1, concat_axis=0, tiled=True)
    members = group_pairs.shape[0]
    group_pairs = group_pairs.reshape(members, kv_heads, tokens_dev, 2 * head_dim)
    head_pairs = jnp.transpose(group_pairs, (1, 0, 2, 3))
    range_len = tokens_dev * seq_count
    blocks_slab = range_len // BLK
    head_queries = head_queries.reshape(range_len, head_dim)
    own_pairs = head_pairs.reshape(range_len, 2 * head_dim)
    own_blocks = own_pairs.reshape(blocks_slab, BLK, 2 * head_dim)
    head_index = lax.axis_index(SEQ)
    range_index = lax.axis_index("ctx")
    vertical = lax.dynamic_index_in_dim(columns, head_index, 0, keepdims=False)
    slashes = lax.dynamic_index_in_dim(offsets, head_index, 0, keepdims=False)
    first_block = range_index * blocks_slab
    owner = vertical // blocks_slab
    earlier = jnp.arange(vertical_count)[None, :] < jnp.arange(vertical_count)[:, None]
    rank = jnp.sum(earlier & (owner[None, :] == owner[:, None]), axis=1)
    rank = jnp.clip(rank, 0, VCAP - 1)
    held = (owner[None, :] == range_index) & (rank[None, :] == jnp.arange(VCAP)[:, None])
    local_index = jnp.sum(jnp.where(held, vertical[None, :] - first_block, 0), axis=1)
    taken_blocks = own_blocks[jnp.clip(local_index, 0, blocks_slab - 1)]
    vertical_pairs = lax.all_gather(taken_blocks, "ctx", tiled=True)
    previous = from_behind(own_pairs[range_len - BACK * BLK :], "ctx", 1)
    key_pool = jnp.concatenate(
        [previous.reshape(BACK, BLK, 2 * head_dim), own_blocks, vertical_pairs], axis=0
    )
    pool_size = key_pool.shape[0]
    pool_base = first_block - BACK
    query_index = first_block + jnp.arange(blocks_slab, dtype=jnp.int32)
    slash_blocks = query_index[:, None] - slashes[None, :]
    repeated = jnp.any(slash_blocks[:, :, None] == vertical[None, None, :], axis=2)
    candidates = jnp.concatenate(
        [jnp.broadcast_to(vertical[None, :], (blocks_slab, vertical_count)), slash_blocks], axis=1
    )
    usable = jnp.concatenate(
        [jnp.ones((blocks_slab, vertical_count), dtype=bool), jnp.logical_not(repeated)], axis=1
    )
    usable = usable & (candidates >= 0) & (candidates <= query_index[:, None])
    strict = candidates < query_index[:, None]
    bounds = jnp.where(usable, jnp.where(strict, BLK, 0), NEVER).astype(jnp.int32)
    vertical_slots = jnp.broadcast_to(
        (BACK + blocks_slab + owner * VCAP + rank).astype(jnp.int32)[None, :],
        (blocks_slab, vertical_count),
    )
    pool_index = jnp.concatenate([vertical_slots, slash_blocks - pool_base], axis=1)
    pool_index = jnp.clip(pool_index, 0, pool_size - 1).astype(jnp.int32)
    head_output = attend(head_queries, key_pool, pool_index, bounds).reshape(range_len, 1, head_dim)
    returned = lax.all_to_all(head_output, SEQ, split_axis=0, concat_axis=1, tiled=True)
    return returned.reshape(1, tokens_dev, seq_count * head_dim)


def solution(mesh):
    def run(queries, keys, values, columns, offsets):
        seq_count = mesh.shape["seq"]
        kv_heads = keys.shape[2] // (queries.shape[2] // seq_count)
        devices = mesh.devices.reshape(kv_heads, seq_count // kv_heads, mesh.shape["ctx"])
        split = Mesh(devices, ("grp", "mem", "ctx"))
        placed = P("ctx", SEQ, None)
        step = jax.shard_map(
            shards,
            mesh=split,
            in_specs=(placed, placed, placed, P(), P()),
            out_specs=placed,
            check_vma=False,
        )
        return step(queries, keys, values, columns, offsets)

    return run
```

```python
import functools
import math

import jax
import jax.numpy as jnp
from jax import lax
from jax.experimental import pallas as pl
from jax.experimental.pallas import tpu as pltpu
from jax.sharding import Mesh, PartitionSpec as P

BLK = 128
SEQ = ("grp", "mem")
BACK = 7
NEVER = -4 * BLK
VCAP = 2


def from_behind(block, axis, distance):
    devices = range(lax.axis_size(axis))
    route = [(i - distance, i) for i in devices if i - distance in devices]
    return lax.ppermute(block, axis, route)


def attend_kernel(
    index_ref, bound_ref, q_ref, pool_ref, o_ref, key_ref, value_ref, *, candidates, head_dim, per_step
):
    step = pl.program_id(0)
    scale = 1.0 / math.sqrt(head_dim)
    row = lax.broadcasted_iota(jnp.int32, (BLK, BLK), 0)
    col = lax.broadcasted_iota(jnp.int32, (BLK, BLK), 1)
    offset = col - row
    for part in range(per_step):
        block = step * per_step + part
        for k in range(candidates):
            slot = index_ref[block * candidates + k]
            key_ref[k * BLK : (k + 1) * BLK, :] = pool_ref[slot, :, :head_dim]
            value_ref[k * BLK : (k + 1) * BLK, :] = pool_ref[slot, :, head_dim:]
        queries = q_ref[part * BLK : (part + 1) * BLK, :]
        scores = (
            lax.dot_general(
                queries, key_ref[...], (((1,), (1,)), ((), ())), preferred_element_type=jnp.float32
            )
            * scale
        )
        masked = []
        for k in range(candidates):
            bound = bound_ref[block * candidates + k]
            masked.append(jnp.where(offset <= bound, scores[:, k * BLK : (k + 1) * BLK], -1e30))
        scores = jnp.concatenate(masked, axis=1)
        row_max = jnp.max(scores, axis=1, keepdims=True)
        weights = jnp.exp(scores - row_max)
        denominator = jnp.sum(weights, axis=1, keepdims=True)
        weighted = jnp.dot(
            weights.astype(jnp.bfloat16), value_ref[...], preferred_element_type=jnp.float32
        )
        o_ref[part * BLK : (part + 1) * BLK, :] = (weighted / denominator).astype(o_ref.dtype)


def attend(head_queries, key_pool, pool_index, bounds, per_step=2):
    range_len, head_dim = head_queries.shape
    blocks = range_len // BLK
    candidates = pool_index.shape[1]
    pool_size = key_pool.shape[0]
    kernel = functools.partial(
        attend_kernel, candidates=candidates, head_dim=head_dim, per_step=per_step
    )
    rows = per_step * BLK
    grid_spec = pltpu.PrefetchScalarGridSpec(
        num_scalar_prefetch=2,
        grid=(blocks // per_step,),
        in_specs=[
            pl.BlockSpec((rows, head_dim), lambda i, *_: (i, 0)),
            pl.BlockSpec((pool_size, BLK, 2 * head_dim), lambda i, *_: (0, 0, 0)),
        ],
        out_specs=pl.BlockSpec((rows, head_dim), lambda i, *_: (i, 0)),
        scratch_shapes=[
            pltpu.VMEM((candidates * BLK, head_dim), jnp.bfloat16),
            pltpu.VMEM((candidates * BLK, head_dim), jnp.bfloat16),
        ],
    )
    flops = 4 * range_len * candidates * BLK * head_dim
    return pl.pallas_call(
        kernel,
        grid_spec=grid_spec,
        out_shape=jax.ShapeDtypeStruct((range_len, head_dim), jnp.bfloat16),
        compiler_params=pltpu.CompilerParams(dimension_semantics=("arbitrary",)),
        cost_estimate=pl.CostEstimate(
            flops=flops,
            transcendentals=range_len * candidates * BLK,
            bytes_accessed=2 * range_len * head_dim * 2 + key_pool.size * 2,
        ),
    )(pool_index.reshape(-1), bounds.reshape(-1), head_queries, key_pool)


def shards(queries, keys, values, columns, offsets):
    tokens_dev = queries.shape[1]
    seq_count = lax.axis_size(SEQ)
    head_dim = queries.shape[2] // seq_count
    kv_heads = keys.shape[2] // head_dim
    vertical_count = columns.shape[1]
    local_queries = queries.reshape(tokens_dev, seq_count, head_dim)
    local_pairs = jnp.concatenate(
        [
            keys.reshape(tokens_dev, kv_heads, head_dim),
            values.reshape(tokens_dev, kv_heads, head_dim),
        ],
        axis=2,
    )
    group_pairs = lax.all_to_all(local_pairs, "grp", split_axis=1, concat_axis=0, tiled=True)
    members = lax.axis_size("mem")
    group_pairs = jnp.broadcast_to(group_pairs[None], (members,) + group_pairs.shape)
    group_pairs = lax.all_to_all(group_pairs, "mem", split_axis=0, concat_axis=0, tiled=True)
    head_queries = lax.all_to_all(local_queries, SEQ, split_axis=1, concat_axis=0, tiled=True)
    group_pairs = group_pairs.reshape(members, kv_heads, tokens_dev, 2 * head_dim)
    head_pairs = jnp.transpose(group_pairs, (1, 0, 2, 3))
    range_len = tokens_dev * seq_count
    blocks_slab = range_len // BLK
    head_queries = head_queries.reshape(range_len, head_dim)
    own_pairs = head_pairs.reshape(range_len, 2 * head_dim)
    own_blocks = own_pairs.reshape(blocks_slab, BLK, 2 * head_dim)
    head_index = lax.axis_index(SEQ)
    range_index = lax.axis_index("ctx")
    vertical = lax.dynamic_index_in_dim(columns, head_index, 0, keepdims=False)
    slashes = lax.dynamic_index_in_dim(offsets, head_index, 0, keepdims=False)
    first_block = range_index * blocks_slab
    owner = vertical // blocks_slab
    earlier = jnp.arange(vertical_count)[None, :] < jnp.arange(vertical_count)[:, None]
    rank = jnp.sum(earlier & (owner[None, :] == owner[:, None]), axis=1)
    rank = jnp.clip(rank, 0, VCAP - 1)
    held = (owner[None, :] == range_index) & (rank[None, :] == jnp.arange(VCAP)[:, None])
    local_index = jnp.sum(jnp.where(held, vertical[None, :] - first_block, 0), axis=1)
    taken_blocks = own_blocks[jnp.clip(local_index, 0, blocks_slab - 1)]
    vertical_pairs = lax.all_gather(taken_blocks, "ctx", tiled=True)
    previous = from_behind(own_pairs[range_len - BACK * BLK :], "ctx", 1)
    key_pool = jnp.concatenate(
        [previous.reshape(BACK, BLK, 2 * head_dim), own_blocks, vertical_pairs], axis=0
    )
    pool_size = key_pool.shape[0]
    pool_base = first_block - BACK
    query_index = first_block + jnp.arange(blocks_slab, dtype=jnp.int32)
    slash_blocks = query_index[:, None] - slashes[None, :]
    repeated = jnp.any(slash_blocks[:, :, None] == vertical[None, None, :], axis=2)
    candidates = jnp.concatenate(
        [jnp.broadcast_to(vertical[None, :], (blocks_slab, vertical_count)), slash_blocks], axis=1
    )
    usable = jnp.concatenate(
        [jnp.ones((blocks_slab, vertical_count), dtype=bool), jnp.logical_not(repeated)], axis=1
    )
    usable = usable & (candidates >= 0) & (candidates <= query_index[:, None])
    strict = candidates < query_index[:, None]
    bounds = jnp.where(usable, jnp.where(strict, BLK, 0), NEVER).astype(jnp.int32)
    vertical_slots = jnp.broadcast_to(
        (BACK + blocks_slab + owner * VCAP + rank).astype(jnp.int32)[None, :],
        (blocks_slab, vertical_count),
    )
    pool_index = jnp.concatenate([vertical_slots, slash_blocks - pool_base], axis=1)
    pool_index = jnp.clip(pool_index, 0, pool_size - 1).astype(jnp.int32)
    head_output = attend(head_queries, key_pool, pool_index, bounds).reshape(range_len, 1, head_dim)
    returned = lax.all_to_all(head_output, SEQ, split_axis=0, concat_axis=1, tiled=True)
    return returned.reshape(1, tokens_dev, seq_count * head_dim)


def solution(mesh):
    def run(queries, keys, values, columns, offsets):
        seq_count = mesh.shape["seq"]
        kv_heads = keys.shape[2] // (queries.shape[2] // seq_count)
        devices = mesh.devices.reshape(kv_heads, seq_count // kv_heads, mesh.shape["ctx"])
        split = Mesh(devices, ("grp", "mem", "ctx"))
        placed = P("ctx", SEQ, None)
        step = jax.shard_map(
            shards,
            mesh=split,
            in_specs=(placed, placed, placed, P(), P()),
            out_specs=placed,
            check_vma=False,
        )
        return step(queries, keys, values, columns, offsets)

    return run
```

```python
import functools
import math

import jax
import jax.numpy as jnp
from jax import lax
from jax.experimental import pallas as pl
from jax.experimental.pallas import tpu as pltpu
from jax.sharding import Mesh, PartitionSpec as P

BLK = 128
SEQ = ("grp", "mem")
BACK = 7
NEVER = -4 * BLK
VCAP = 2


def from_behind(block, axis, distance):
    devices = range(lax.axis_size(axis))
    route = [(i - distance, i) for i in devices if i - distance in devices]
    return lax.ppermute(block, axis, route)


def attend_kernel(
    index_ref, bound_ref, q_ref, pool_ref, o_ref, key_ref, value_ref, *, candidates, head_dim, per_step
):
    step = pl.program_id(0)
    scale = 1.0 / math.sqrt(head_dim)
    row = lax.broadcasted_iota(jnp.int32, (BLK, BLK), 0)
    col = lax.broadcasted_iota(jnp.int32, (BLK, BLK), 1)
    offset = col - row
    for part in range(per_step):
        block = step * per_step + part
        for k in range(candidates):
            slot = index_ref[block * candidates + k]
            key_ref[k * BLK : (k + 1) * BLK, :] = pool_ref[slot, :, :head_dim]
            value_ref[k * BLK : (k + 1) * BLK, :] = pool_ref[slot, :, head_dim:]
        queries = q_ref[part * BLK : (part + 1) * BLK, :]
        scores = (
            lax.dot_general(
                queries, key_ref[...], (((1,), (1,)), ((), ())), preferred_element_type=jnp.float32
            )
            * scale
        )
        masked = []
        for k in range(candidates):
            bound = bound_ref[block * candidates + k]
            masked.append(jnp.where(offset <= bound, scores[:, k * BLK : (k + 1) * BLK], -1e30))
        scores = jnp.concatenate(masked, axis=1)
        row_max = jnp.max(scores, axis=1, keepdims=True)
        weights = jnp.exp(scores - row_max)
        denominator = jnp.sum(weights, axis=1, keepdims=True)
        weighted = jnp.dot(
            weights.astype(jnp.bfloat16), value_ref[...], preferred_element_type=jnp.float32
        )
        o_ref[part * BLK : (part + 1) * BLK, :] = (weighted / denominator).astype(o_ref.dtype)


def attend(head_queries, key_pool, pool_index, bounds, per_step=2):
    range_len, head_dim = head_queries.shape
    blocks = range_len // BLK
    candidates = pool_index.shape[1]
    pool_size = key_pool.shape[0]
    kernel = functools.partial(
        attend_kernel, candidates=candidates, head_dim=head_dim, per_step=per_step
    )
    rows = per_step * BLK
    grid_spec = pltpu.PrefetchScalarGridSpec(
        num_scalar_prefetch=2,
        grid=(blocks // per_step,),
        in_specs=[
            pl.BlockSpec((rows, head_dim), lambda i, *_: (i, 0)),
            pl.BlockSpec((pool_size, BLK, 2 * head_dim), lambda i, *_: (0, 0, 0)),
        ],
        out_specs=pl.BlockSpec((rows, head_dim), lambda i, *_: (i, 0)),
        scratch_shapes=[
            pltpu.VMEM((candidates * BLK, head_dim), jnp.bfloat16),
            pltpu.VMEM((candidates * BLK, head_dim), jnp.bfloat16),
        ],
    )
    flops = 4 * range_len * candidates * BLK * head_dim
    return pl.pallas_call(
        kernel,
        grid_spec=grid_spec,
        out_shape=jax.ShapeDtypeStruct((range_len, head_dim), jnp.bfloat16),
        compiler_params=pltpu.CompilerParams(dimension_semantics=("arbitrary",)),
        cost_estimate=pl.CostEstimate(
            flops=flops,
            transcendentals=range_len * candidates * BLK,
            bytes_accessed=2 * range_len * head_dim * 2 + key_pool.size * 2,
        ),
    )(pool_index.reshape(-1), bounds.reshape(-1), head_queries, key_pool)


def shards(queries, keys, values, columns, offsets):
    tokens_dev = queries.shape[1]
    seq_count = lax.axis_size(SEQ)
    head_dim = queries.shape[2] // seq_count
    kv_heads = keys.shape[2] // head_dim
    vertical_count = columns.shape[1]
    local_queries = queries.reshape(tokens_dev, seq_count, head_dim)
    local_pairs = jnp.concatenate(
        [
            keys.reshape(tokens_dev, kv_heads, head_dim),
            values.reshape(tokens_dev, kv_heads, head_dim),
        ],
        axis=2,
    )
    groups = lax.axis_size("grp")
    group = lax.axis_index("grp")
    sent = [jnp.take(local_pairs, group, axis=1)]
    for distance in range(1, groups):
        route = [(i, (i + distance) % groups) for i in range(groups)]
        piece = jnp.take(local_pairs, (group + distance) % groups, axis=1)
        sent.append(lax.ppermute(piece, "grp", route))
    group_pairs = jnp.stack(sent)[(group - jnp.arange(groups, dtype=jnp.int32)) % groups]
    group_pairs = group_pairs.reshape(groups * tokens_dev, 1, 2 * head_dim)
    members = lax.axis_size("mem")
    shifted = [group_pairs]
    for distance in range(1, members):
        route = [(i, (i + distance) % members) for i in range(members)]
        shifted.append(lax.ppermute(group_pairs, "mem", route))
    member = lax.axis_index("mem")
    order = (member - jnp.arange(members, dtype=jnp.int32)) % members
    group_pairs = jnp.stack(shifted)[order]
    head_queries = lax.all_to_all(local_queries, SEQ, split_axis=1, concat_axis=0, tiled=True)
    group_pairs = group_pairs.reshape(members, kv_heads, tokens_dev, 2 * head_dim)
    head_pairs = jnp.transpose(group_pairs, (1, 0, 2, 3))
    range_len = tokens_dev * seq_count
    blocks_slab = range_len // BLK
    head_queries = head_queries.reshape(range_len, head_dim)
    own_pairs = head_pairs.reshape(range_len, 2 * head_dim)
    own_blocks = own_pairs.reshape(blocks_slab, BLK, 2 * head_dim)
    head_index = lax.axis_index(SEQ)
    range_index = lax.axis_index("ctx")
    vertical = lax.dynamic_index_in_dim(columns, head_index, 0, keepdims=False)
    slashes = lax.dynamic_index_in_dim(offsets, head_index, 0, keepdims=False)
    first_block = range_index * blocks_slab
    owner = vertical // blocks_slab
    earlier = jnp.arange(vertical_count)[None, :] < jnp.arange(vertical_count)[:, None]
    rank = jnp.sum(earlier & (owner[None, :] == owner[:, None]), axis=1)
    rank = jnp.clip(rank, 0, VCAP - 1)
    held = (owner[None, :] == range_index) & (rank[None, :] == jnp.arange(VCAP)[:, None])
    local_index = jnp.sum(jnp.where(held, vertical[None, :] - first_block, 0), axis=1)
    taken_blocks = own_blocks[jnp.clip(local_index, 0, blocks_slab - 1)]
    vertical_pairs = lax.all_gather(taken_blocks, "ctx", tiled=True)
    previous = from_behind(own_pairs[range_len - BACK * BLK :], "ctx", 1)
    key_pool = jnp.concatenate(
        [previous.reshape(BACK, BLK, 2 * head_dim), own_blocks, vertical_pairs], axis=0
    )
    pool_size = key_pool.shape[0]
    pool_base = first_block - BACK
    query_index = first_block + jnp.arange(blocks_slab, dtype=jnp.int32)
    slash_blocks = query_index[:, None] - slashes[None, :]
    repeated = jnp.any(slash_blocks[:, :, None] == vertical[None, None, :], axis=2)
    candidates = jnp.concatenate(
        [jnp.broadcast_to(vertical[None, :], (blocks_slab, vertical_count)), slash_blocks], axis=1
    )
    usable = jnp.concatenate(
        [jnp.ones((blocks_slab, vertical_count), dtype=bool), jnp.logical_not(repeated)], axis=1
    )
    usable = usable & (candidates >= 0) & (candidates <= query_index[:, None])
    strict = candidates < query_index[:, None]
    bounds = jnp.where(usable, jnp.where(strict, BLK, 0), NEVER).astype(jnp.int32)
    vertical_slots = jnp.broadcast_to(
        (BACK + blocks_slab + owner * VCAP + rank).astype(jnp.int32)[None, :],
        (blocks_slab, vertical_count),
    )
    pool_index = jnp.concatenate([vertical_slots, slash_blocks - pool_base], axis=1)
    pool_index = jnp.clip(pool_index, 0, pool_size - 1).astype(jnp.int32)
    head_output = attend(head_queries, key_pool, pool_index, bounds).reshape(range_len, 1, head_dim)
    returned = lax.all_to_all(head_output, SEQ, split_axis=0, concat_axis=1, tiled=True)
    return returned.reshape(1, tokens_dev, seq_count * head_dim)


def solution(mesh):
    def run(queries, keys, values, columns, offsets):
        seq_count = mesh.shape["seq"]
        kv_heads = keys.shape[2] // (queries.shape[2] // seq_count)
        devices = mesh.devices.reshape(kv_heads, seq_count // kv_heads, mesh.shape["ctx"])
        split = Mesh(devices, ("grp", "mem", "ctx"))
        placed = P("ctx", SEQ, None)
        step = jax.shard_map(
            shards,
            mesh=split,
            in_specs=(placed, placed, placed, P(), P()),
            out_specs=placed,
            check_vma=False,
        )
        return step(queries, keys, values, columns, offsets)

    return run
```

```python
import functools
import math

import jax
import jax.numpy as jnp
from jax import lax
from jax.experimental import pallas as pl
from jax.experimental.pallas import tpu as pltpu
from jax.sharding import Mesh, PartitionSpec as P

BLK = 128
SEQ = ("grp", "mem")
BACK = 7
NEVER = -4 * BLK
VCAP = 2


def from_behind(block, axis, distance):
    devices = range(lax.axis_size(axis))
    route = [(i - distance, i) for i in devices if i - distance in devices]
    return lax.ppermute(block, axis, route)


def attend_kernel(
    index_ref, bound_ref, q_ref, pool_ref, o_ref, key_ref, value_ref, *, candidates, head_dim, per_step
):
    step = pl.program_id(0)
    scale = 1.0 / math.sqrt(head_dim)
    row = lax.broadcasted_iota(jnp.int32, (BLK, BLK), 0)
    col = lax.broadcasted_iota(jnp.int32, (BLK, BLK), 1)
    offset = col - row
    for part in range(per_step):
        block = step * per_step + part
        for k in range(candidates):
            slot = index_ref[block * candidates + k]
            key_ref[k * BLK : (k + 1) * BLK, :] = pool_ref[slot, :, :head_dim]
            value_ref[k * BLK : (k + 1) * BLK, :] = pool_ref[slot, :, head_dim:]
        queries = q_ref[part * BLK : (part + 1) * BLK, :]
        scores = (
            lax.dot_general(
                queries, key_ref[...], (((1,), (1,)), ((), ())), preferred_element_type=jnp.float32
            )
            * scale
        )
        masked = []
        for k in range(candidates):
            bound = bound_ref[block * candidates + k]
            masked.append(jnp.where(offset <= bound, scores[:, k * BLK : (k + 1) * BLK], -1e30))
        scores = jnp.concatenate(masked, axis=1)
        row_max = jnp.max(scores, axis=1, keepdims=True)
        weights = jnp.exp(scores - row_max)
        denominator = jnp.sum(weights, axis=1, keepdims=True)
        weighted = jnp.dot(
            weights.astype(jnp.bfloat16), value_ref[...], preferred_element_type=jnp.float32
        )
        o_ref[part * BLK : (part + 1) * BLK, :] = (weighted / denominator).astype(o_ref.dtype)


def attend(head_queries, key_pool, pool_index, bounds, per_step=4):
    range_len, head_dim = head_queries.shape
    blocks = range_len // BLK
    candidates = pool_index.shape[1]
    pool_size = key_pool.shape[0]
    kernel = functools.partial(
        attend_kernel, candidates=candidates, head_dim=head_dim, per_step=per_step
    )
    rows = per_step * BLK
    grid_spec = pltpu.PrefetchScalarGridSpec(
        num_scalar_prefetch=2,
        grid=(blocks // per_step,),
        in_specs=[
            pl.BlockSpec((rows, head_dim), lambda i, *_: (i, 0)),
            pl.BlockSpec((pool_size, BLK, 2 * head_dim), lambda i, *_: (0, 0, 0)),
        ],
        out_specs=pl.BlockSpec((rows, head_dim), lambda i, *_: (i, 0)),
        scratch_shapes=[
            pltpu.VMEM((candidates * BLK, head_dim), jnp.bfloat16),
            pltpu.VMEM((candidates * BLK, head_dim), jnp.bfloat16),
        ],
    )
    flops = 4 * range_len * candidates * BLK * head_dim
    return pl.pallas_call(
        kernel,
        grid_spec=grid_spec,
        out_shape=jax.ShapeDtypeStruct((range_len, head_dim), jnp.bfloat16),
        compiler_params=pltpu.CompilerParams(dimension_semantics=("arbitrary",)),
        cost_estimate=pl.CostEstimate(
            flops=flops,
            transcendentals=range_len * candidates * BLK,
            bytes_accessed=2 * range_len * head_dim * 2 + key_pool.size * 2,
        ),
    )(pool_index.reshape(-1), bounds.reshape(-1), head_queries, key_pool)


def shards(queries, keys, values, columns, offsets):
    tokens_dev = queries.shape[1]
    seq_count = lax.axis_size(SEQ)
    head_dim = queries.shape[2] // seq_count
    kv_heads = keys.shape[2] // head_dim
    vertical_count = columns.shape[1]
    local_queries = queries.reshape(tokens_dev, seq_count, head_dim)
    local_pairs = jnp.concatenate(
        [
            keys.reshape(tokens_dev, kv_heads, head_dim),
            values.reshape(tokens_dev, kv_heads, head_dim),
        ],
        axis=2,
    )
    group_pairs = lax.all_to_all(local_pairs, "grp", split_axis=1, concat_axis=0, tiled=True)
    members = lax.axis_size("mem")
    group_pairs = jnp.broadcast_to(group_pairs[None], (members,) + group_pairs.shape)
    group_pairs = lax.all_to_all(group_pairs, "mem", split_axis=0, concat_axis=0, tiled=True)
    head_queries = lax.all_to_all(local_queries, SEQ, split_axis=1, concat_axis=0, tiled=True)
    group_pairs = group_pairs.reshape(members, kv_heads, tokens_dev, 2 * head_dim)
    head_pairs = jnp.transpose(group_pairs, (1, 0, 2, 3))
    range_len = tokens_dev * seq_count
    blocks_slab = range_len // BLK
    head_queries = head_queries.reshape(range_len, head_dim)
    own_pairs = head_pairs.reshape(range_len, 2 * head_dim)
    own_blocks = own_pairs.reshape(blocks_slab, BLK, 2 * head_dim)
    head_index = lax.axis_index(SEQ)
    range_index = lax.axis_index("ctx")
    vertical = lax.dynamic_index_in_dim(columns, head_index, 0, keepdims=False)
    slashes = lax.dynamic_index_in_dim(offsets, head_index, 0, keepdims=False)
    first_block = range_index * blocks_slab
    owner = vertical // blocks_slab
    earlier = jnp.arange(vertical_count)[None, :] < jnp.arange(vertical_count)[:, None]
    rank = jnp.sum(earlier & (owner[None, :] == owner[:, None]), axis=1)
    rank = jnp.clip(rank, 0, VCAP - 1)
    held = (owner[None, :] == range_index) & (rank[None, :] == jnp.arange(VCAP)[:, None])
    local_index = jnp.sum(jnp.where(held, vertical[None, :] - first_block, 0), axis=1)
    taken_blocks = own_blocks[jnp.clip(local_index, 0, blocks_slab - 1)]
    vertical_pairs = lax.all_gather(taken_blocks, "ctx", tiled=True)
    previous = from_behind(own_pairs[range_len - BACK * BLK :], "ctx", 1)
    key_pool = jnp.concatenate(
        [previous.reshape(BACK, BLK, 2 * head_dim), own_blocks, vertical_pairs], axis=0
    )
    pool_size = key_pool.shape[0]
    pool_base = first_block - BACK
    query_index = first_block + jnp.arange(blocks_slab, dtype=jnp.int32)
    slash_blocks = query_index[:, None] - slashes[None, :]
    repeated = jnp.any(slash_blocks[:, :, None] == vertical[None, None, :], axis=2)
    candidates = jnp.concatenate(
        [jnp.broadcast_to(vertical[None, :], (blocks_slab, vertical_count)), slash_blocks], axis=1
    )
    usable = jnp.concatenate(
        [jnp.ones((blocks_slab, vertical_count), dtype=bool), jnp.logical_not(repeated)], axis=1
    )
    usable = usable & (candidates >= 0) & (candidates <= query_index[:, None])
    strict = candidates < query_index[:, None]
    bounds = jnp.where(usable, jnp.where(strict, BLK, 0), NEVER).astype(jnp.int32)
    vertical_slots = jnp.broadcast_to(
        (BACK + blocks_slab + owner * VCAP + rank).astype(jnp.int32)[None, :],
        (blocks_slab, vertical_count),
    )
    pool_index = jnp.concatenate([vertical_slots, slash_blocks - pool_base], axis=1)
    pool_index = jnp.clip(pool_index, 0, pool_size - 1).astype(jnp.int32)
    head_output = attend(head_queries, key_pool, pool_index, bounds)
    head_output = head_output.reshape(seq_count, tokens_dev, head_dim)
    returned = lax.all_to_all(head_output, SEQ, split_axis=0, concat_axis=0, tiled=True)
    returned = jnp.transpose(returned, (1, 0, 2))
    return returned.reshape(1, tokens_dev, seq_count * head_dim)


def solution(mesh):
    def run(queries, keys, values, columns, offsets):
        seq_count = mesh.shape["seq"]
        kv_heads = keys.shape[2] // (queries.shape[2] // seq_count)
        devices = mesh.devices.reshape(kv_heads, seq_count // kv_heads, mesh.shape["ctx"])
        split = Mesh(devices, ("grp", "mem", "ctx"))
        placed = P("ctx", SEQ, None)
        step = jax.shard_map(
            shards,
            mesh=split,
            in_specs=(placed, placed, placed, P(), P()),
            out_specs=placed,
            check_vma=False,
        )
        return step(queries, keys, values, columns, offsets)

    return run
```

```python
import functools
import math

import jax
import jax.numpy as jnp
from jax import lax
from jax.experimental import pallas as pl
from jax.experimental.pallas import tpu as pltpu
from jax.sharding import Mesh, PartitionSpec as P

BLK = 128
SEQ = ("grp", "mem")
BACK = 7
NEVER = -4 * BLK
VCAP = 2


def from_behind(block, axis, distance):
    devices = range(lax.axis_size(axis))
    route = [(i - distance, i) for i in devices if i - distance in devices]
    return lax.ppermute(block, axis, route)


def attend_kernel(
    index_ref, bound_ref, q_ref, pool_ref, o_ref, key_ref, value_ref, *, candidates, head_dim, per_step
):
    step = pl.program_id(0)
    scale = 1.0 / math.sqrt(head_dim)
    row = lax.broadcasted_iota(jnp.int32, (BLK, BLK), 0)
    col = lax.broadcasted_iota(jnp.int32, (BLK, BLK), 1)
    offset = col - row
    for part in range(per_step):
        block = step * per_step + part
        for k in range(candidates):
            slot = index_ref[block * candidates + k]
            key_ref[k * BLK : (k + 1) * BLK, :] = pool_ref[slot, :, :head_dim]
            value_ref[k * BLK : (k + 1) * BLK, :] = pool_ref[slot, :, head_dim:]
        queries = q_ref[part * BLK : (part + 1) * BLK, :]
        scores = (
            lax.dot_general(
                key_ref[...], queries, (((1,), (1,)), ((), ())), preferred_element_type=jnp.float32
            )
            * scale
        )
        masked = []
        for k in range(candidates):
            bound = bound_ref[block * candidates + k]
            masked.append(jnp.where(-offset <= bound, scores[k * BLK : (k + 1) * BLK, :], -1e30))
        scores = jnp.concatenate(masked, axis=0)
        col_max = jnp.max(scores, axis=0, keepdims=True)
        weights = jnp.exp(scores - col_max)
        denominator = jnp.sum(weights, axis=0, keepdims=True)
        weighted = lax.dot_general(
            weights.astype(jnp.bfloat16),
            value_ref[...],
            (((0,), (0,)), ((), ())),
            preferred_element_type=jnp.float32,
        )
        result = (weighted.T / denominator).astype(o_ref.dtype)
        o_ref[part * BLK : (part + 1) * BLK, :] = result.T


def attend(head_queries, key_pool, pool_index, bounds, per_step=4):
    range_len, head_dim = head_queries.shape
    blocks = range_len // BLK
    candidates = pool_index.shape[1]
    pool_size = key_pool.shape[0]
    kernel = functools.partial(
        attend_kernel, candidates=candidates, head_dim=head_dim, per_step=per_step
    )
    rows = per_step * BLK
    grid_spec = pltpu.PrefetchScalarGridSpec(
        num_scalar_prefetch=2,
        grid=(blocks // per_step,),
        in_specs=[
            pl.BlockSpec((rows, head_dim), lambda i, *_: (i, 0)),
            pl.BlockSpec((pool_size, BLK, 2 * head_dim), lambda i, *_: (0, 0, 0)),
        ],
        out_specs=pl.BlockSpec((rows, head_dim), lambda i, *_: (i, 0)),
        scratch_shapes=[
            pltpu.VMEM((candidates * BLK, head_dim), jnp.bfloat16),
            pltpu.VMEM((candidates * BLK, head_dim), jnp.bfloat16),
        ],
    )
    flops = 4 * range_len * candidates * BLK * head_dim
    return pl.pallas_call(
        kernel,
        grid_spec=grid_spec,
        out_shape=jax.ShapeDtypeStruct((range_len, head_dim), jnp.bfloat16),
        compiler_params=pltpu.CompilerParams(dimension_semantics=("arbitrary",)),
        cost_estimate=pl.CostEstimate(
            flops=flops,
            transcendentals=range_len * candidates * BLK,
            bytes_accessed=2 * range_len * head_dim * 2 + key_pool.size * 2,
        ),
    )(pool_index.reshape(-1), bounds.reshape(-1), head_queries, key_pool)


def shards(queries, keys, values, columns, offsets):
    tokens_dev = queries.shape[1]
    seq_count = lax.axis_size(SEQ)
    head_dim = queries.shape[2] // seq_count
    kv_heads = keys.shape[2] // head_dim
    vertical_count = columns.shape[1]
    local_queries = queries.reshape(tokens_dev, seq_count, head_dim)
    local_pairs = jnp.concatenate(
        [
            keys.reshape(tokens_dev, kv_heads, head_dim),
            values.reshape(tokens_dev, kv_heads, head_dim),
        ],
        axis=2,
    )
    group_pairs = lax.all_to_all(local_pairs, "grp", split_axis=1, concat_axis=0, tiled=True)
    members = lax.axis_size("mem")
    group_pairs = jnp.broadcast_to(group_pairs[None], (members,) + group_pairs.shape)
    group_pairs = lax.all_to_all(group_pairs, "mem", split_axis=0, concat_axis=0, tiled=True)
    head_queries = lax.all_to_all(local_queries, SEQ, split_axis=1, concat_axis=0, tiled=True)
    group_pairs = group_pairs.reshape(members, kv_heads, tokens_dev, 2 * head_dim)
    head_pairs = jnp.transpose(group_pairs, (1, 0, 2, 3))
    range_len = tokens_dev * seq_count
    blocks_slab = range_len // BLK
    head_queries = head_queries.reshape(range_len, head_dim)
    own_pairs = head_pairs.reshape(range_len, 2 * head_dim)
    own_blocks = own_pairs.reshape(blocks_slab, BLK, 2 * head_dim)
    head_index = lax.axis_index(SEQ)
    range_index = lax.axis_index("ctx")
    vertical = lax.dynamic_index_in_dim(columns, head_index, 0, keepdims=False)
    slashes = lax.dynamic_index_in_dim(offsets, head_index, 0, keepdims=False)
    first_block = range_index * blocks_slab
    owner = vertical // blocks_slab
    earlier = jnp.arange(vertical_count)[None, :] < jnp.arange(vertical_count)[:, None]
    rank = jnp.sum(earlier & (owner[None, :] == owner[:, None]), axis=1)
    rank = jnp.clip(rank, 0, VCAP - 1)
    held = (owner[None, :] == range_index) & (rank[None, :] == jnp.arange(VCAP)[:, None])
    local_index = jnp.sum(jnp.where(held, vertical[None, :] - first_block, 0), axis=1)
    taken_blocks = own_blocks[jnp.clip(local_index, 0, blocks_slab - 1)]
    vertical_pairs = lax.all_gather(taken_blocks, "ctx", tiled=True)
    previous = from_behind(own_pairs[range_len - BACK * BLK :], "ctx", 1)
    key_pool = jnp.concatenate(
        [previous.reshape(BACK, BLK, 2 * head_dim), own_blocks, vertical_pairs], axis=0
    )
    pool_size = key_pool.shape[0]
    pool_base = first_block - BACK
    query_index = first_block + jnp.arange(blocks_slab, dtype=jnp.int32)
    slash_blocks = query_index[:, None] - slashes[None, :]
    repeated = jnp.any(slash_blocks[:, :, None] == vertical[None, None, :], axis=2)
    candidates = jnp.concatenate(
        [jnp.broadcast_to(vertical[None, :], (blocks_slab, vertical_count)), slash_blocks], axis=1
    )
    usable = jnp.concatenate(
        [jnp.ones((blocks_slab, vertical_count), dtype=bool), jnp.logical_not(repeated)], axis=1
    )
    usable = usable & (candidates >= 0) & (candidates <= query_index[:, None])
    strict = candidates < query_index[:, None]
    bounds = jnp.where(usable, jnp.where(strict, BLK, 0), NEVER).astype(jnp.int32)
    vertical_slots = jnp.broadcast_to(
        (BACK + blocks_slab + owner * VCAP + rank).astype(jnp.int32)[None, :],
        (blocks_slab, vertical_count),
    )
    pool_index = jnp.concatenate([vertical_slots, slash_blocks - pool_base], axis=1)
    pool_index = jnp.clip(pool_index, 0, pool_size - 1).astype(jnp.int32)
    head_output = attend(head_queries, key_pool, pool_index, bounds)
    head_output = head_output.reshape(seq_count, tokens_dev, head_dim)
    returned = lax.all_to_all(head_output, SEQ, split_axis=0, concat_axis=0, tiled=True)
    returned = jnp.transpose(returned, (1, 0, 2))
    return returned.reshape(1, tokens_dev, seq_count * head_dim)


def solution(mesh):
    def run(queries, keys, values, columns, offsets):
        seq_count = mesh.shape["seq"]
        kv_heads = keys.shape[2] // (queries.shape[2] // seq_count)
        devices = mesh.devices.reshape(kv_heads, seq_count // kv_heads, mesh.shape["ctx"])
        split = Mesh(devices, ("grp", "mem", "ctx"))
        placed = P("ctx", SEQ, None)
        step = jax.shard_map(
            shards,
            mesh=split,
            in_specs=(placed, placed, placed, P(), P()),
            out_specs=placed,
            check_vma=False,
        )
        return step(queries, keys, values, columns, offsets)

    return run
```

```python
import functools
import math

import jax
import jax.numpy as jnp
from jax import lax
from jax.experimental import pallas as pl
from jax.experimental.pallas import tpu as pltpu
from jax.sharding import Mesh, PartitionSpec as P

BLK = 128
SEQ = ("grp", "mem")
BACK = 7
NEVER = -4 * BLK
VCAP = 2


def from_behind(block, axis, distance):
    devices = range(lax.axis_size(axis))
    route = [(i - distance, i) for i in devices if i - distance in devices]
    return lax.ppermute(block, axis, route)


def attend_kernel(
    index_ref, bound_ref, q_ref, pool_ref, o_ref, key_ref, value_ref, *, candidates, head_dim, per_step
):
    step = pl.program_id(0)
    scale = 1.0 / math.sqrt(head_dim)
    row = lax.broadcasted_iota(jnp.int32, (BLK, BLK), 0)
    col = lax.broadcasted_iota(jnp.int32, (BLK, BLK), 1)
    offset = col - row
    for part in range(per_step):
        block = step * per_step + part
        for k in range(candidates):
            slot = index_ref[block * candidates + k]
            key_ref[k * BLK : (k + 1) * BLK, :] = pool_ref[slot, :, :head_dim]
            value_ref[k * BLK : (k + 1) * BLK, :] = pool_ref[slot, :, head_dim:]
        queries = q_ref[part * BLK : (part + 1) * BLK, :]
        scores = (
            lax.dot_general(
                queries, key_ref[...], (((1,), (1,)), ((), ())), preferred_element_type=jnp.float32
            )
            * scale
        )
        masked = []
        for k in range(candidates):
            bound = bound_ref[block * candidates + k]
            masked.append(jnp.where(offset <= bound, scores[:, k * BLK : (k + 1) * BLK], -1e30))
        scores = jnp.concatenate(masked, axis=1)
        row_max = jnp.max(scores, axis=1, keepdims=True)
        weights = jnp.exp(scores - row_max)
        denominator = jnp.sum(weights, axis=1, keepdims=True)
        weighted = jnp.dot(
            weights.astype(jnp.bfloat16), value_ref[...], preferred_element_type=jnp.float32
        )
        o_ref[part * BLK : (part + 1) * BLK, :] = (weighted / denominator).astype(o_ref.dtype)


def attend(head_queries, key_pool, pool_index, bounds, per_step=8):
    range_len, head_dim = head_queries.shape
    blocks = range_len // BLK
    candidates = pool_index.shape[1]
    pool_size = key_pool.shape[0]
    kernel = functools.partial(
        attend_kernel, candidates=candidates, head_dim=head_dim, per_step=per_step
    )
    rows = per_step * BLK
    grid_spec = pltpu.PrefetchScalarGridSpec(
        num_scalar_prefetch=2,
        grid=(blocks // per_step,),
        in_specs=[
            pl.BlockSpec((rows, head_dim), lambda i, *_: (i, 0)),
            pl.BlockSpec((pool_size, BLK, 2 * head_dim), lambda i, *_: (0, 0, 0)),
        ],
        out_specs=pl.BlockSpec((rows, head_dim), lambda i, *_: (i, 0)),
        scratch_shapes=[
            pltpu.VMEM((candidates * BLK, head_dim), jnp.bfloat16),
            pltpu.VMEM((candidates * BLK, head_dim), jnp.bfloat16),
        ],
    )
    flops = 4 * range_len * candidates * BLK * head_dim
    return pl.pallas_call(
        kernel,
        grid_spec=grid_spec,
        out_shape=jax.ShapeDtypeStruct((range_len, head_dim), jnp.bfloat16),
        compiler_params=pltpu.CompilerParams(dimension_semantics=("arbitrary",)),
        cost_estimate=pl.CostEstimate(
            flops=flops,
            transcendentals=range_len * candidates * BLK,
            bytes_accessed=2 * range_len * head_dim * 2 + key_pool.size * 2,
        ),
    )(pool_index.reshape(-1), bounds.reshape(-1), head_queries, key_pool)


def shards(queries, keys, values, columns, offsets):
    tokens_dev = queries.shape[1]
    seq_count = lax.axis_size(SEQ)
    head_dim = queries.shape[2] // seq_count
    kv_heads = keys.shape[2] // head_dim
    vertical_count = columns.shape[1]
    local_queries = queries.reshape(tokens_dev, seq_count, head_dim)
    local_pairs = jnp.concatenate(
        [
            keys.reshape(tokens_dev, kv_heads, head_dim),
            values.reshape(tokens_dev, kv_heads, head_dim),
        ],
        axis=2,
    )
    group_pairs = lax.all_to_all(local_pairs, "grp", split_axis=1, concat_axis=0, tiled=True)
    members = lax.axis_size("mem")
    groups = group_pairs.shape[0] // tokens_dev
    group_pairs = group_pairs.reshape(1, groups, 1, tokens_dev, 2 * head_dim)
    group_pairs = jnp.broadcast_to(group_pairs, (members,) + group_pairs.shape[1:])
    head_pairs = lax.all_to_all(group_pairs, "mem", split_axis=0, concat_axis=2, tiled=True)
    head_queries = lax.all_to_all(local_queries, SEQ, split_axis=1, concat_axis=0, tiled=True)
    range_len = tokens_dev * seq_count
    blocks_slab = range_len // BLK
    head_queries = head_queries.reshape(range_len, head_dim)
    own_pairs = head_pairs.reshape(range_len, 2 * head_dim)
    own_blocks = own_pairs.reshape(blocks_slab, BLK, 2 * head_dim)
    head_index = lax.axis_index(SEQ)
    range_index = lax.axis_index("ctx")
    vertical = lax.dynamic_index_in_dim(columns, head_index, 0, keepdims=False)
    slashes = lax.dynamic_index_in_dim(offsets, head_index, 0, keepdims=False)
    first_block = range_index * blocks_slab
    owner = vertical // blocks_slab
    earlier = jnp.arange(vertical_count)[None, :] < jnp.arange(vertical_count)[:, None]
    rank = jnp.sum(earlier & (owner[None, :] == owner[:, None]), axis=1)
    rank = jnp.clip(rank, 0, VCAP - 1)
    held = (owner[None, :] == range_index) & (rank[None, :] == jnp.arange(VCAP)[:, None])
    local_index = jnp.sum(jnp.where(held, vertical[None, :] - first_block, 0), axis=1)
    taken_blocks = own_blocks[jnp.clip(local_index, 0, blocks_slab - 1)]
    vertical_pairs = lax.all_gather(taken_blocks, "ctx", tiled=True)
    previous = from_behind(own_pairs[range_len - BACK * BLK :], "ctx", 1)
    key_pool = jnp.concatenate(
        [previous.reshape(BACK, BLK, 2 * head_dim), own_blocks, vertical_pairs], axis=0
    )
    pool_size = key_pool.shape[0]
    pool_base = first_block - BACK
    query_index = first_block + jnp.arange(blocks_slab, dtype=jnp.int32)
    slash_blocks = query_index[:, None] - slashes[None, :]
    repeated = jnp.any(slash_blocks[:, :, None] == vertical[None, None, :], axis=2)
    candidates = jnp.concatenate(
        [jnp.broadcast_to(vertical[None, :], (blocks_slab, vertical_count)), slash_blocks], axis=1
    )
    usable = jnp.concatenate(
        [jnp.ones((blocks_slab, vertical_count), dtype=bool), jnp.logical_not(repeated)], axis=1
    )
    usable = usable & (candidates >= 0) & (candidates <= query_index[:, None])
    strict = candidates < query_index[:, None]
    bounds = jnp.where(usable, jnp.where(strict, BLK, 0), NEVER).astype(jnp.int32)
    vertical_slots = jnp.broadcast_to(
        (BACK + blocks_slab + owner * VCAP + rank).astype(jnp.int32)[None, :],
        (blocks_slab, vertical_count),
    )
    pool_index = jnp.concatenate([vertical_slots, slash_blocks - pool_base], axis=1)
    pool_index = jnp.clip(pool_index, 0, pool_size - 1).astype(jnp.int32)
    head_output = attend(head_queries, key_pool, pool_index, bounds)
    head_output = head_output.reshape(seq_count, tokens_dev, head_dim)
    returned = lax.all_to_all(head_output, SEQ, split_axis=0, concat_axis=0, tiled=True)
    returned = jnp.transpose(returned, (1, 0, 2))
    return returned.reshape(1, tokens_dev, seq_count * head_dim)


def solution(mesh):
    def run(queries, keys, values, columns, offsets):
        seq_count = mesh.shape["seq"]
        kv_heads = keys.shape[2] // (queries.shape[2] // seq_count)
        devices = mesh.devices.reshape(kv_heads, seq_count // kv_heads, mesh.shape["ctx"])
        split = Mesh(devices, ("grp", "mem", "ctx"))
        placed = P("ctx", SEQ, None)
        step = jax.shard_map(
            shards,
            mesh=split,
            in_specs=(placed, placed, placed, P(), P()),
            out_specs=placed,
            check_vma=False,
        )
        return step(queries, keys, values, columns, offsets)

    return run
```
